512 devices in a mesh: gx: 32 (over x, z), gy: 16 (over y, core).
Axes of the slice: x: 4, y: 8, z: 8, core: 2. Of those that a mesh axis runs over, the one named last changes fastest.
Arguments:
- sources: float32 [1024, 512, 192], P('gx', 'gy'), may hold values from -12 to 12
- permeability: float32 [1024, 512], P('gx', 'gy'), may hold values from 0.2 to 5
- storage: float32 [1024, 512], P('gx', 'gy'), may hold values from 0.05 to 1
- basis: float32 [8, 1024, 512], P(None, 'gx', 'gy'), may hold values from -0.3 to 0.3
- local_inverse: bfloat16 [32, 16, 1024, 1600], P('gx', 'gy'), may hold values from -0.2 to 0.4
- coarse_inverse: float32 [4096, 4096], P(('gx', 'gy')), may hold values from -1.2 to 2.2
Outputs:
- solution: float32 [1024, 512, 192], P('gx', 'gy')
- residual_norms: float32 [3, 192], replicated
- initial_norms: float32 [192], replicated
The draws below stay inside these ranges and needn't reach their ends.
All inputs are finite; a program needn't handle non-finite values.
Results may differ from the reference program's by a relative error of at most 0.0007.
Values may be sent and summed in bfloat16 or wider, within the bound.
No kernel may reach another device: no remote copies, remote signals or barrier semaphores. Data moves between devices by JAX's collectives and lax.ppermute only.
A program may use at most 64 MiB of HBM per device.

```python
import math
import jax
import jax.numpy as jnp
from jax import lax

P_SIZE = 32
OV = 4
MODES = 8
S = 192
ITERS = 3
NPX = 32
NPY = 16
NPATCH = 512
NC = 4096
NX = 1024
NY = 512


locality = 6.0


def draw_sources(key, part):
    noise_key = jax.random.fold_in(key, 0)
    along_x = jnp.arange(NX, dtype=jnp.float32) / float(max(NX - 1, 1))
    growth = (1.0 + 2.0 * along_x)[:, None, None]
    return jax.random.truncated_normal(noise_key, -3.0, 3.0, (NX, NY, S)) * growth


def draw_local_inverse(key, part):
    width = P_SIZE + 2 * OV
    cells = jnp.arange(P_SIZE * P_SIZE, dtype=jnp.int32)
    row_first = cells // P_SIZE + OV
    row_second = cells % P_SIZE + OV
    columns = jnp.arange(width * width, dtype=jnp.int32)
    col_first = columns // width
    col_second = columns % width
    squared = (row_first[:, None] - col_first[None, :]) ** 2 + (row_second[:, None] - col_second[None, :]) ** 2
    envelope = jnp.exp(-jnp.sqrt(squared.astype(jnp.float32)) / locality)
    centre_mask = jnp.where(squared == 0, 1.0, 0.0)

    def patch_row(row_number):
        row_key = jax.random.fold_in(key, row_number)
        noise_key, diag_key = jax.random.split(row_key)
        noise = jnp.clip(jax.random.normal(noise_key, (NPY, P_SIZE * P_SIZE, width * width)), -5.0, 5.0)
        diagonal = jax.random.uniform(diag_key, (NPY, P_SIZE * P_SIZE, 1), minval=0.08, maxval=0.2)
        result = 0.03 * envelope[None] * noise + centre_mask[None] * diagonal
        return result.astype(jnp.bfloat16)
    return lax.map(patch_row, jnp.arange(NPX, dtype=jnp.int32))


def draw_coarse_inverse(key, part):
    dense_key, partner_key, strong_key, diag_key = jax.random.split(key, 4)
    dense = jnp.clip(jax.random.normal(dense_key, (NC, NC)), -5.0, 5.0) * (0.3 / math.sqrt(NC))
    partner = jax.random.permutation(partner_key, NPATCH)
    owner = jnp.arange(NC, dtype=jnp.int32) // MODES
    strong_mask = jnp.where(partner[owner][:, None] == owner[None, :], 1.0, 0.0)
    strong = jnp.clip(jax.random.normal(strong_key, (NC, NC)), -5.0, 5.0) * (0.6 / math.sqrt(MODES)) * strong_mask
    diagonal = jax.random.uniform(diag_key, (NC,), minval=0.5, maxval=1.0)
    return dense + strong + jnp.diag(diagonal)


def block_levels(own_key, dims, cuts, low, high):
    gain = 1.0
    for axis_at, blocks in cuts:
        steps = jax.random.uniform(jax.random.fold_in(jax.random.fold_in(own_key, 6), axis_at), (blocks,), jnp.float32, low / len(cuts), high / len(cuts))
        gain = gain * jnp.repeat(jnp.exp(steps), dims[axis_at] // blocks).reshape((-1,) + (1,) * (len(dims) - 1 - axis_at))
    return gain


def scatter_about(rng, dims, scale, most, cuts=(), held_as=jnp.bfloat16):
    gain = block_levels(rng, dims, cuts, -0.22, 0.18) if cuts else 1.0
    values = jax.random.normal(rng, dims, jnp.float32) * scale * gain
    return jnp.minimum(jnp.maximum(values, -most), most).astype(held_as)


def setup_inputs(seed: int = 0) -> dict:
    seeds = jax.random.split(jax.random.key(seed), 7)
    sources = draw_sources(jax.random.fold_in(seeds[6], 71), 0)
    permeability = jnp.clip(jnp.exp(math.log(5.0) - 3.218876 * jax.random.uniform(seeds[1], (NX, NY), jnp.float32) ** block_levels(seeds[1], (NX, NY), ((0, 32), (1, 16)), -0.2, 0.2)), 0.2, 5.0)
    storage = jnp.clip(jnp.exp(math.log(1.0) - 2.9957323 * jax.random.uniform(seeds[2], (NX, NY), jnp.float32) ** block_levels(seeds[2], (NX, NY), ((0, 32), (1, 16)), -0.2, 0.2)), 0.05, 1.0)
    basis = scatter_about(seeds[3], (MODES, NX, NY), 0.05, 0.3, ((1, 32), (2, 16)), jnp.float32)
    local_inverse = draw_local_inverse(jax.random.fold_in(seeds[6], 71), 0)
    coarse_inverse = draw_coarse_inverse(jax.random.fold_in(seeds[6], 71), 0)
    return {"sources": sources, "permeability": permeability, "storage": storage, "basis": basis, "local_inverse": local_inverse, "coarse_inverse": coarse_inverse}


lower_bound = 0.15
upper_bound = 1.9
highest = lax.Precision.HIGHEST

def neighbour(padded, offset_row, offset_col):
    inner_rows = padded.shape[0] - 2
    inner_cols = padded.shape[1] - 2
    return padded[1 + offset_row:1 + offset_row + inner_rows, 1 + offset_col:1 + offset_col + inner_cols]

def operate(field_pad, kappa_pad, storage_used):
    centre = neighbour(field_pad, 0, 0)
    kappa = neighbour(kappa_pad, 0, 0)
    total = storage_used[:, :, None] * centre
    for offset_row, offset_col in ((1, 0), (-1, 0), (0, 1), (0, -1)):
        faces = 0.5 * (kappa + neighbour(kappa_pad, offset_row, offset_col))
        total = total + faces[:, :, None] * (centre - neighbour(field_pad, offset_row, offset_col))
    return total

def local_solve(residual, local_inverse):
    extent = P_SIZE + 2 * OV
    padded = jnp.pad(residual, ((OV, OV), (OV, OV), (0, 0)))

    def patch_row(row_number):
        block = lax.dynamic_slice_in_dim(padded, row_number * P_SIZE, extent, 0)
        starts = jnp.arange(NPY, dtype=jnp.int32) * P_SIZE
        windows = jax.vmap(lambda begin: lax.dynamic_slice_in_dim(block, begin, extent, 1))(starts)
        rounded = lax.optimization_barrier(windows.astype(jnp.bfloat16)).astype(jnp.float32)
        rounded = rounded.reshape(NPY, extent * extent, S)
        inverse_rows = local_inverse[row_number].astype(jnp.float32)
        product = jnp.einsum('bcq,bqs->bcs', inverse_rows, rounded, precision=highest)
        return product.reshape(NPY, P_SIZE, P_SIZE, S).transpose(1, 0, 2, 3).reshape(P_SIZE, NY, S)
    stacked_rows = lax.map(patch_row, jnp.arange(NPX, dtype=jnp.int32))
    return stacked_rows.reshape(NX, NY, S)

def precondition(residual, basis, local_inverse, coarse_inverse):
    local_part = local_solve(residual, local_inverse)
    basis_blocks = basis.reshape(MODES, NPX, P_SIZE, NPY, P_SIZE)
    field_blocks = residual.reshape(NPX, P_SIZE, NPY, P_SIZE, S)
    coarse_residual = jnp.einsum('maibj,aibjs->abms', basis_blocks, field_blocks, precision=highest).reshape(NC, S)
    coarse_solution = jnp.dot(coarse_inverse, coarse_residual, precision=highest)
    prolonged = jnp.einsum('maibj,abms->aibjs', basis_blocks, coarse_solution.reshape(NPX, NPY, MODES, S), precision=highest)
    return local_part + prolonged.reshape(NX, NY, S)

def reference(sources, permeability, storage, basis, local_inverse, coarse_inverse):
    kappa_pad = jnp.pad(permeability, 1)

    def apply_operator(field):
        return operate(jnp.pad(field, ((1, 1), (1, 1), (0, 0))), kappa_pad, storage)

    def squares(field):
        return lax.optimization_barrier(jnp.sum(field * field, axis=(0, 1)))
    centre = 0.5 * (upper_bound + lower_bound)
    half_width = 0.5 * (upper_bound - lower_bound)
    relative = centre / half_width
    weight_prev = 1.0 / relative
    solution = jnp.zeros_like(sources)
    residual = sources
    initial = squares(residual)
    history = []
    update = precondition(residual, basis, local_inverse, coarse_inverse) / centre
    for index in range(ITERS):
        solution = solution + update
        residual = residual - apply_operator(update)
        history.append(squares(residual))
        if index + 1 < ITERS:
            corrected = precondition(residual, basis, local_inverse, coarse_inverse)
            weight_next = 1.0 / (2.0 * relative - weight_prev)
            update = weight_next * weight_prev * update + 2.0 * weight_next / half_width * corrected
            weight_prev = weight_next
    cells = float(NX * NY)
    return (solution, jnp.sqrt(jnp.stack(history) / cells), jnp.sqrt(initial / cells))
```

```python
import jax
import jax.numpy as jnp
from jax import lax
from jax.sharding import PartitionSpec as P

OV = 4
ITERS = 3


lower_bound = 0.15
upper_bound = 1.9
highest = lax.Precision.HIGHEST


def extended(cells, sides, width):
    for axis, dim in sides:
        count = lax.axis_size(axis)
        ends = count - 1
        head = lax.slice_in_dim(cells, 0, width, axis=dim)
        tail = lax.slice_in_dim(cells, cells.shape[dim] - width, cells.shape[dim], axis=dim)
        cells = jnp.concatenate(
            [
                lax.ppermute(tail, axis, [(i, (i + 1) % count) for i in range(ends)]),
                cells,
                lax.ppermute(head, axis, [((i + 1) % count, i) for i in range(ends)]),
            ],
            axis=dim,
        )
    return cells


def neighbour(padded, offset_row, offset_col):
    inner_rows = padded.shape[0] - 2
    inner_cols = padded.shape[1] - 2
    return padded[
        1 + offset_row : 1 + offset_row + inner_rows, 1 + offset_col : 1 + offset_col + inner_cols
    ]


def operate(field_pad, kappa_pad, storage_used):
    centre = neighbour(field_pad, 0, 0)
    kappa = neighbour(kappa_pad, 0, 0)
    total = storage_used[:, :, None] * centre
    for offset_row, offset_col in ((1, 0), (-1, 0), (0, 1), (0, -1)):
        faces = 0.5 * (kappa + neighbour(kappa_pad, offset_row, offset_col))
        total = total + faces[:, :, None] * (centre - neighbour(field_pad, offset_row, offset_col))
    return total


def total_over_mesh(values):
    for axis in ("gx", "gy"):
        values = jnp.sum(lax.all_gather(values, axis, axis=0), axis=0)
    return values


def on_device(sources, permeability, storage, basis, local_inverse, coarse_inverse):
    patch = sources.shape[0]
    fields = sources.shape[2]
    modes = basis.shape[0]
    rows_x = lax.axis_size("gx")
    cols_y = lax.axis_size("gy")
    margin = OV
    extent = patch + 2 * margin
    cells = float(patch * patch * rows_x * cols_y)
    flat_basis = basis.reshape(modes, patch * patch)
    inverse_rows = local_inverse[0, 0]
    stacked = jnp.stack([permeability, storage])
    padded = extended(stacked, (("gx", 1), ("gy", 2)), 1)
    kappa_pad = padded[0]
    state = sources

    pieces = coarse_inverse.reshape(modes, rows_x, cols_y, modes).transpose(2, 0, 1, 3)
    pieces = lax.all_to_all(pieces, "gy", 0, 0, tiled=True)
    coarse_block = pieces.reshape(cols_y * modes, rows_x * modes)

    def rounded_window(current):
        return extended(current.astype(jnp.bfloat16), (("gx", 0), ("gy", 1)), margin)

    def precondition(current):
        window = rounded_window(current).reshape(extent * extent, fields)
        local_part = jnp.dot(inverse_rows, window, preferred_element_type=jnp.float32).reshape(
            patch, patch, fields
        )
        flat_core = current.reshape(patch * patch, fields)
        restricted = jnp.dot(flat_basis, flat_core, precision=highest)
        squares = jnp.sum(flat_core * flat_core, axis=0)
        carried = jnp.concatenate([restricted, squares[None]], axis=0)
        gathered = lax.all_gather(carried, "gx", axis=0)
        column_total = jnp.sum(gathered[:, modes], axis=0)
        column_coarse = gathered[:, :modes].reshape(rows_x * modes, fields)
        partial = jnp.dot(coarse_block, column_coarse, precision=highest).reshape(
            cols_y, modes, fields
        )
        partial = jnp.concatenate(
            [partial, jnp.broadcast_to(column_total, (cols_y, 1, fields))], axis=1
        )
        reduced = lax.psum_scatter(partial, "gy", scatter_dimension=0, tiled=True)[0]
        coarse_part = reduced[:modes]
        squares_all = reduced[modes]
        prolonged = jnp.dot(flat_basis.T, coarse_part, precision=highest).reshape(
            patch, patch, fields
        )
        return (local_part + prolonged, squares_all)

    centre = 0.5 * (upper_bound + lower_bound)
    half_width = 0.5 * (upper_bound - lower_bound)
    relative = centre / half_width
    weight_prev = 1.0 / relative
    solution = jnp.zeros_like(sources)
    corrected, initial = precondition(state)
    history = []
    update = corrected / centre
    for index in range(ITERS):
        solution = solution + update
        step_pad = extended(update, (("gx", 0), ("gy", 1)), 1)
        state = state - operate(step_pad, kappa_pad, storage)
        if index + 1 < ITERS:
            corrected, squares = precondition(state)
            history.append(squares)
            weight_next = 1.0 / (2.0 * relative - weight_prev)
            update = weight_next * weight_prev * update + 2.0 * weight_next / half_width * corrected
            weight_prev = weight_next
        else:
            flat_state = state.reshape(patch * patch, fields)
            history.append(total_over_mesh(jnp.sum(flat_state * flat_state, axis=0)))
    return (solution, jnp.sqrt(jnp.stack(history) / cells), jnp.sqrt(initial / cells))


def solution(mesh):
    placed = (
        P("gx", "gy", None),
        P("gx", "gy"),
        P("gx", "gy"),
        P(None, "gx", "gy"),
        P("gx", "gy", None, None),
        P(("gx", "gy"), None),
    )
    return jax.shard_map(
        on_device,
        mesh=mesh,
        in_specs=placed,
        out_specs=(P("gx", "gy", None), P(), P()),
        check_vma=False,
    )
```

```python
import jax
import jax.numpy as jnp
from jax import lax
from jax.sharding import PartitionSpec as P

OV = 4
ITERS = 3


lower_bound = 0.15
upper_bound = 1.9
highest = lax.Precision.HIGHEST


def extended(cells, sides, width):
    for axis, dim in sides:
        count = lax.axis_size(axis)
        ends = count - 1
        head = lax.slice_in_dim(cells, 0, width, axis=dim)
        tail = lax.slice_in_dim(cells, cells.shape[dim] - width, cells.shape[dim], axis=dim)
        cells = jnp.concatenate(
            [
                lax.ppermute(tail, axis, [(i, (i + 1) % count) for i in range(ends)]),
                cells,
                lax.ppermute(head, axis, [((i + 1) % count, i) for i in range(ends)]),
            ],
            axis=dim,
        )
    return cells


def neighbour(padded, offset_row, offset_col):
    inner_rows = padded.shape[0] - 2
    inner_cols = padded.shape[1] - 2
    return padded[
        1 + offset_row : 1 + offset_row + inner_rows, 1 + offset_col : 1 + offset_col + inner_cols
    ]


def operate(field_pad, kappa_pad, storage_used):
    centre = neighbour(field_pad, 0, 0)
    kappa = neighbour(kappa_pad, 0, 0)
    total = storage_used[:, :, None] * centre
    for offset_row, offset_col in ((1, 0), (-1, 0), (0, 1), (0, -1)):
        faces = 0.5 * (kappa + neighbour(kappa_pad, offset_row, offset_col))
        total = total + faces[:, :, None] * (centre - neighbour(field_pad, offset_row, offset_col))
    return total


def exchange(values, axis, distance):
    count = lax.axis_size(axis)
    return lax.ppermute(values, axis, [(i, i ^ distance) for i in range(count)])


def gather_by_doubling(block, axis):
    count = lax.axis_size(axis)
    me = lax.axis_index(axis)
    held = block
    distance = 1
    while distance < count:
        other = exchange(held, axis, distance)
        upper = (me // distance) % 2 == 1
        held = jnp.where(
            upper, jnp.concatenate([other, held], axis=0), jnp.concatenate([held, other], axis=0)
        )
        distance *= 2
    return held


def scatter_by_halving(blocks, extra, axis):
    count = lax.axis_size(axis)
    me = lax.axis_index(axis)
    tail = blocks.shape[1:]
    distance = 1
    while distance < count:
        pairs = blocks.reshape((blocks.shape[0] // 2, 2) + tail)
        upper = (me // distance) % 2 == 1
        keep = jnp.where(upper, pairs[:, 1], pairs[:, 0])
        send = jnp.where(upper, pairs[:, 0], pairs[:, 1])
        message = jnp.concatenate([send.reshape((-1,) + tail[1:]), extra[None]], axis=0)
        other = exchange(message, axis, distance)
        blocks = keep + other[:-1].reshape(keep.shape)
        extra = extra + other[-1]
        distance *= 2
    return blocks[0], extra


def total_by_doubling(values, axis):
    count = lax.axis_size(axis)
    distance = 1
    while distance < count:
        values = values + exchange(values, axis, distance)
        distance *= 2
    return values


def total_over_mesh(values):
    for axis in ("gy", "gx"):
        values = total_by_doubling(values, axis)
    return values


def on_device(sources, permeability, storage, basis, local_inverse, coarse_inverse):
    patch = sources.shape[0]
    fields = sources.shape[2]
    modes = basis.shape[0]
    rows_x = lax.axis_size("gx")
    cols_y = lax.axis_size("gy")
    margin = OV
    extent = patch + 2 * margin
    cells = float(patch * patch * rows_x * cols_y)
    flat_basis = basis.reshape(modes, patch * patch)
    inverse_rows = local_inverse[0, 0]
    stacked = jnp.stack([permeability, storage])
    padded = extended(stacked, (("gx", 1), ("gy", 2)), 1)
    kappa_pad = padded[0]
    state = sources

    pieces = coarse_inverse.reshape(modes, rows_x, cols_y, modes).transpose(2, 0, 1, 3)
    pieces = lax.all_to_all(pieces, "gy", 0, 0, tiled=True)
    coarse_block = pieces.reshape(cols_y * modes, rows_x * modes)

    def rounded_window(current):
        return extended(current.astype(jnp.bfloat16), (("gx", 0), ("gy", 1)), margin)

    def precondition(current):
        window = rounded_window(current).reshape(extent * extent, fields)
        local_part = jnp.dot(inverse_rows, window, preferred_element_type=jnp.float32).reshape(
            patch, patch, fields
        )
        flat_core = current.reshape(patch * patch, fields)
        restricted = jnp.dot(flat_basis, flat_core, precision=highest)
        squares = jnp.sum(flat_core * flat_core, axis=0)
        carried = jnp.concatenate([restricted, squares[None]], axis=0)
        gathered = gather_by_doubling(carried[None], "gx")
        column_total = jnp.sum(gathered[:, modes], axis=0)
        column_coarse = gathered[:, :modes].reshape(rows_x * modes, fields)
        partial = jnp.dot(coarse_block, column_coarse, precision=highest).reshape(
            cols_y, modes, fields
        )
        coarse_part, squares_all = scatter_by_halving(partial, column_total, "gy")
        prolonged = jnp.dot(flat_basis.T, coarse_part, precision=highest).reshape(
            patch, patch, fields
        )
        return (local_part + prolonged, squares_all)

    centre = 0.5 * (upper_bound + lower_bound)
    half_width = 0.5 * (upper_bound - lower_bound)
    relative = centre / half_width
    weight_prev = 1.0 / relative
    solution = jnp.zeros_like(sources)
    corrected, initial = precondition(state)
    history = []
    update = corrected / centre
    for index in range(ITERS):
        solution = solution + update
        step_pad = extended(update, (("gx", 0), ("gy", 1)), 1)
        state = state - operate(step_pad, kappa_pad, storage)
        if index + 1 < ITERS:
            corrected, squares = precondition(state)
            history.append(squares)
            weight_next = 1.0 / (2.0 * relative - weight_prev)
            update = weight_next * weight_prev * update + 2.0 * weight_next / half_width * corrected
            weight_prev = weight_next
        else:
            flat_state = state.reshape(patch * patch, fields)
            history.append(total_over_mesh(jnp.sum(flat_state * flat_state, axis=0)))
    return (solution, jnp.sqrt(jnp.stack(history) / cells), jnp.sqrt(initial / cells))


def solution(mesh):
    placed = (
        P("gx", "gy", None),
        P("gx", "gy"),
        P("gx", "gy"),
        P(None, "gx", "gy"),
        P("gx", "gy", None, None),
        P(("gx", "gy"), None),
    )
    return jax.shard_map(
        on_device,
        mesh=mesh,
        in_specs=placed,
        out_specs=(P("gx", "gy", None), P(), P()),
        check_vma=False,
    )
```

```python
import jax
import jax.numpy as jnp
from jax import lax
from jax.sharding import PartitionSpec as P

OV = 4
ITERS = 3


lower_bound = 0.15
upper_bound = 1.9
highest = lax.Precision.HIGHEST


def extended(cells, sides, width):
    for axis, dim in sides:
        count = lax.axis_size(axis)
        ends = count - 1
        head = lax.slice_in_dim(cells, 0, width, axis=dim)
        tail = lax.slice_in_dim(cells, cells.shape[dim] - width, cells.shape[dim], axis=dim)
        cells = jnp.concatenate(
            [
                lax.ppermute(tail, axis, [(i, (i + 1) % count) for i in range(ends)]),
                cells,
                lax.ppermute(head, axis, [((i + 1) % count, i) for i in range(ends)]),
            ],
            axis=dim,
        )
    return cells


def neighbour(padded, offset_row, offset_col):
    inner_rows = padded.shape[0] - 2
    inner_cols = padded.shape[1] - 2
    return padded[
        1 + offset_row : 1 + offset_row + inner_rows, 1 + offset_col : 1 + offset_col + inner_cols
    ]


def operate(field_pad, kappa_pad, storage_used):
    centre = neighbour(field_pad, 0, 0)
    kappa = neighbour(kappa_pad, 0, 0)
    total = storage_used[:, :, None] * centre
    for offset_row, offset_col in ((1, 0), (-1, 0), (0, 1), (0, -1)):
        faces = 0.5 * (kappa + neighbour(kappa_pad, offset_row, offset_col))
        total = total + faces[:, :, None] * (centre - neighbour(field_pad, offset_row, offset_col))
    return total


def gathered_by_exchange(block, axis):
    count = lax.axis_size(axis)
    copies = jnp.broadcast_to(block[None], (count,) + block.shape)
    return lax.all_to_all(copies, axis, 0, 0, tiled=True)


def summed_by_exchange(blocks, axis):
    return jnp.sum(lax.all_to_all(blocks, axis, 0, 0, tiled=True), axis=0)


def total_over_mesh(values):
    for axis in ("gy", "gx"):
        values = jnp.sum(gathered_by_exchange(values, axis), axis=0)
    return values


def on_device(sources, permeability, storage, basis, local_inverse, coarse_inverse):
    patch = sources.shape[0]
    fields = sources.shape[2]
    modes = basis.shape[0]
    rows_x = lax.axis_size("gx")
    cols_y = lax.axis_size("gy")
    margin = OV
    extent = patch + 2 * margin
    cells = float(patch * patch * rows_x * cols_y)
    flat_basis = basis.reshape(modes, patch * patch)
    inverse_rows = local_inverse[0, 0]
    stacked = jnp.stack([permeability, storage])
    padded = extended(stacked, (("gx", 1), ("gy", 2)), 1)
    kappa_pad = padded[0]
    state = sources

    pieces = coarse_inverse.reshape(modes, rows_x, cols_y, modes).transpose(2, 0, 1, 3)
    pieces = lax.all_to_all(pieces, "gy", 0, 0, tiled=True)
    coarse_block = pieces.reshape(cols_y * modes, rows_x * modes)

    def rounded_window(current):
        return extended(current.astype(jnp.bfloat16), (("gx", 0), ("gy", 1)), margin)

    def precondition(current):
        window = rounded_window(current).reshape(extent * extent, fields)
        local_part = jnp.dot(inverse_rows, window, preferred_element_type=jnp.float32).reshape(
            patch, patch, fields
        )
        flat_core = current.reshape(patch * patch, fields)
        restricted = jnp.dot(flat_basis, flat_core, precision=highest)
        squares = jnp.sum(flat_core * flat_core, axis=0)
        carried = jnp.concatenate([restricted, squares[None]], axis=0)
        gathered = gathered_by_exchange(carried, "gx")
        column_total = jnp.sum(gathered[:, modes], axis=0)
        column_coarse = gathered[:, :modes].reshape(rows_x * modes, fields)
        partial = jnp.dot(coarse_block, column_coarse, precision=highest).reshape(
            cols_y, modes, fields
        )
        partial = jnp.concatenate(
            [partial, jnp.broadcast_to(column_total, (cols_y, 1, fields))], axis=1
        )
        reduced = summed_by_exchange(partial, "gy")
        coarse_part = reduced[:modes]
        squares_all = reduced[modes]
        prolonged = jnp.dot(flat_basis.T, coarse_part, precision=highest).reshape(
            patch, patch, fields
        )
        return (local_part + prolonged, squares_all)

    centre = 0.5 * (upper_bound + lower_bound)
    half_width = 0.5 * (upper_bound - lower_bound)
    relative = centre / half_width
    weight_prev = 1.0 / relative
    solution = jnp.zeros_like(sources)
    corrected, initial = precondition(state)
    history = []
    update = corrected / centre
    for index in range(ITERS):
        solution = solution + update
        step_pad = extended(update, (("gx", 0), ("gy", 1)), 1)
        state = state - operate(step_pad, kappa_pad, storage)
        if index + 1 < ITERS:
            corrected, squares = precondition(state)
            history.append(squares)
            weight_next = 1.0 / (2.0 * relative - weight_prev)
            update = weight_next * weight_prev * update + 2.0 * weight_next / half_width * corrected
            weight_prev = weight_next
        else:
            flat_state = state.reshape(patch * patch, fields)
            history.append(total_over_mesh(jnp.sum(flat_state * flat_state, axis=0)))
    return (solution, jnp.sqrt(jnp.stack(history) / cells), jnp.sqrt(initial / cells))


def solution(mesh):
    placed = (
        P("gx", "gy", None),
        P("gx", "gy"),
        P("gx", "gy"),
        P(None, "gx", "gy"),
        P("gx", "gy", None, None),
        P(("gx", "gy"), None),
    )
    return jax.shard_map(
        on_device,
        mesh=mesh,
        in_specs=placed,
        out_specs=(P("gx", "gy", None), P(), P()),
        check_vma=False,
    )
```

```python
import jax
import jax.numpy as jnp
from jax import lax
from jax.sharding import PartitionSpec as P

OV = 4
ITERS = 3


lower_bound = 0.15
upper_bound = 1.9
highest = lax.Precision.HIGHEST


def extended(cells, sides, width):
    for axis, dim in sides:
        count = lax.axis_size(axis)
        ends = count - 1
        head = lax.slice_in_dim(cells, 0, width, axis=dim)
        tail = lax.slice_in_dim(cells, cells.shape[dim] - width, cells.shape[dim], axis=dim)
        cells = jnp.concatenate(
            [
                lax.ppermute(tail, axis, [(i, (i + 1) % count) for i in range(ends)]),
                cells,
                lax.ppermute(head, axis, [((i + 1) % count, i) for i in range(ends)]),
            ],
            axis=dim,
        )
    return cells


def with_edges(cells):
    rows_x = lax.axis_size("gx")
    cols_y = lax.axis_size("gy")
    down = [(i, i + 1) for i in range(rows_x - 1)]
    up = [(i + 1, i) for i in range(rows_x - 1)]
    right = [(i, i + 1) for i in range(cols_y - 1)]
    left = [(i + 1, i) for i in range(cols_y - 1)]
    north = lax.ppermute(cells[-1:], "gx", down)
    south = lax.ppermute(cells[:1], "gx", up)
    west = lax.ppermute(cells[:, -1:], "gy", right)
    east = lax.ppermute(cells[:, :1], "gy", left)
    rows = jnp.concatenate([north, cells, south], axis=0)
    corner = [(1, 1), (0, 0)] + [(0, 0)] * (cells.ndim - 2)
    return jnp.concatenate(
        [jnp.pad(west, corner), rows, jnp.pad(east, corner)], axis=1
    )


def neighbour(padded, offset_row, offset_col):
    inner_rows = padded.shape[0] - 2
    inner_cols = padded.shape[1] - 2
    return padded[
        1 + offset_row : 1 + offset_row + inner_rows, 1 + offset_col : 1 + offset_col + inner_cols
    ]


def operate(field_pad, kappa_pad, storage_used):
    centre = neighbour(field_pad, 0, 0)
    kappa = neighbour(kappa_pad, 0, 0)
    total = storage_used[:, :, None] * centre
    for offset_row, offset_col in ((1, 0), (-1, 0), (0, 1), (0, -1)):
        faces = 0.5 * (kappa + neighbour(kappa_pad, offset_row, offset_col))
        total = total + faces[:, :, None] * (centre - neighbour(field_pad, offset_row, offset_col))
    return total


def gathered_by_exchange(block, axis):
    count = lax.axis_size(axis)
    copies = jnp.broadcast_to(block[None], (count,) + block.shape)
    return lax.all_to_all(copies, axis, 0, 0, tiled=True)


def summed_by_exchange(blocks, axis):
    return jnp.sum(lax.all_to_all(blocks, axis, 0, 0, tiled=True), axis=0)


def total_over_mesh(values):
    return jnp.sum(gathered_by_exchange(values, ("gx", "gy")), axis=0)


def on_device(sources, permeability, storage, basis, local_inverse, coarse_inverse):
    patch = sources.shape[0]
    fields = sources.shape[2]
    modes = basis.shape[0]
    rows_x = lax.axis_size("gx")
    cols_y = lax.axis_size("gy")
    margin = OV
    extent = patch + 2 * margin
    cells = float(patch * patch * rows_x * cols_y)
    flat_basis = basis.reshape(modes, patch * patch)
    inverse_rows = local_inverse[0, 0]
    kappa_pad = with_edges(permeability)
    state = sources

    pieces = coarse_inverse.reshape(modes, rows_x, cols_y, modes).transpose(2, 0, 1, 3)
    pieces = lax.all_to_all(pieces, "gy", 0, 0, tiled=True)
    coarse_block = pieces.reshape(cols_y * modes, rows_x * modes)

    def rounded_window(current):
        return extended(current.astype(jnp.bfloat16), (("gx", 0), ("gy", 1)), margin)

    def precondition(current):
        window = rounded_window(current).reshape(extent * extent, fields)
        local_part = jnp.dot(inverse_rows, window, preferred_element_type=jnp.float32).reshape(
            patch, patch, fields
        )
        flat_core = current.reshape(patch * patch, fields)
        restricted = jnp.dot(flat_basis, flat_core, precision=highest)
        squares = jnp.sum(flat_core * flat_core, axis=0)
        carried = jnp.concatenate([restricted, squares[None]], axis=0)
        gathered = gathered_by_exchange(carried, "gx")
        column_total = jnp.sum(gathered[:, modes], axis=0)
        column_coarse = gathered[:, :modes].reshape(rows_x * modes, fields)
        partial = jnp.dot(coarse_block, column_coarse, precision=highest).reshape(
            cols_y, modes, fields
        )
        partial = jnp.concatenate(
            [partial, jnp.broadcast_to(column_total, (cols_y, 1, fields))], axis=1
        )
        reduced = summed_by_exchange(partial, "gy")
        coarse_part = reduced[:modes]
        squares_all = reduced[modes]
        prolonged = jnp.dot(flat_basis.T, coarse_part, precision=highest).reshape(
            patch, patch, fields
        )
        return (local_part + prolonged, squares_all)

    centre = 0.5 * (upper_bound + lower_bound)
    half_width = 0.5 * (upper_bound - lower_bound)
    relative = centre / half_width
    weight_prev = 1.0 / relative
    solution = jnp.zeros_like(sources)
    corrected, initial = precondition(state)
    history = []
    update = corrected / centre
    for index in range(ITERS):
        solution = solution + update
        step_pad = with_edges(update)
        state = state - operate(step_pad, kappa_pad, storage)
        if index + 1 < ITERS:
            corrected, squares = precondition(state)
            history.append(squares)
            weight_next = 1.0 / (2.0 * relative - weight_prev)
            update = weight_next * weight_prev * update + 2.0 * weight_next / half_width * corrected
            weight_prev = weight_next
        else:
            flat_state = state.reshape(patch * patch, fields)
            history.append(total_over_mesh(jnp.sum(flat_state * flat_state, axis=0)))
    return (solution, jnp.sqrt(jnp.stack(history) / cells), jnp.sqrt(initial / cells))


def solution(mesh):
    placed = (
        P("gx", "gy", None),
        P("gx", "gy"),
        P("gx", "gy"),
        P(None, "gx", "gy"),
        P("gx", "gy", None, None),
        P(("gx", "gy"), None),
    )
    return jax.shard_map(
        on_device,
        mesh=mesh,
        in_specs=placed,
        out_specs=(P("gx", "gy", None), P(), P()),
        check_vma=False,
    )
```

```python
import jax
import jax.numpy as jnp
from jax import lax
from jax.sharding import PartitionSpec as P

OV = 4
ITERS = 3


lower_bound = 0.15
upper_bound = 1.9
highest = lax.Precision.HIGHEST


def extended(cells, sides, width):
    for axis, dim in sides:
        count = lax.axis_size(axis)
        ends = count - 1
        head = lax.slice_in_dim(cells, 0, width, axis=dim)
        tail = lax.slice_in_dim(cells, cells.shape[dim] - width, cells.shape[dim], axis=dim)
        cells = jnp.concatenate(
            [
                lax.ppermute(tail, axis, [(i, (i + 1) % count) for i in range(ends)]),
                cells,
                lax.ppermute(head, axis, [((i + 1) % count, i) for i in range(ends)]),
            ],
            axis=dim,
        )
    return cells


def with_edges(cells):
    rows_x = lax.axis_size("gx")
    cols_y = lax.axis_size("gy")
    down = [(i, i + 1) for i in range(rows_x - 1)]
    up = [(i + 1, i) for i in range(rows_x - 1)]
    right = [(i, i + 1) for i in range(cols_y - 1)]
    left = [(i + 1, i) for i in range(cols_y - 1)]
    north = lax.ppermute(cells[-1:], "gx", down)
    south = lax.ppermute(cells[:1], "gx", up)
    west = lax.ppermute(cells[:, -1:], "gy", right)
    east = lax.ppermute(cells[:, :1], "gy", left)
    rows = jnp.concatenate([north, cells, south], axis=0)
    corner = [(1, 1), (0, 0)] + [(0, 0)] * (cells.ndim - 2)
    return jnp.concatenate(
        [jnp.pad(west, corner), rows, jnp.pad(east, corner)], axis=1
    )


def neighbour(padded, offset_row, offset_col):
    inner_rows = padded.shape[0] - 2
    inner_cols = padded.shape[1] - 2
    return padded[
        1 + offset_row : 1 + offset_row + inner_rows, 1 + offset_col : 1 + offset_col + inner_cols
    ]


def operate(field_pad, kappa_pad, storage_used):
    centre = neighbour(field_pad, 0, 0)
    kappa = neighbour(kappa_pad, 0, 0)
    total = storage_used[:, :, None] * centre
    for offset_row, offset_col in ((1, 0), (-1, 0), (0, 1), (0, -1)):
        faces = 0.5 * (kappa + neighbour(kappa_pad, offset_row, offset_col))
        total = total + faces[:, :, None] * (centre - neighbour(field_pad, offset_row, offset_col))
    return total


def gathered_by_exchange(block, axis):
    count = lax.axis_size(axis)
    flat = block.reshape(-1)
    copies = jnp.broadcast_to(flat[None], (count, flat.shape[0]))
    return lax.all_to_all(copies, axis, 0, 0, tiled=True).reshape((count,) + block.shape)


def summed_by_exchange(blocks, axis):
    count = blocks.shape[0]
    flat = blocks.reshape(count, -1)
    received = lax.all_to_all(flat, axis, 0, 0, tiled=True)
    return jnp.sum(received, axis=0).reshape(blocks.shape[1:])


def total_over_mesh(values):
    return jnp.sum(gathered_by_exchange(values, ("gx", "gy")), axis=0)


def on_device(sources, permeability, storage, basis, local_inverse, coarse_inverse):
    patch = sources.shape[0]
    fields = sources.shape[2]
    modes = basis.shape[0]
    rows_x = lax.axis_size("gx")
    cols_y = lax.axis_size("gy")
    margin = OV
    extent = patch + 2 * margin
    cells = float(patch * patch * rows_x * cols_y)
    flat_basis = basis.reshape(modes, patch * patch)
    inverse_rows = local_inverse[0, 0]
    kappa_pad = with_edges(permeability)
    state = sources

    pieces = coarse_inverse.reshape(modes, rows_x, cols_y, modes).transpose(2, 0, 1, 3)
    pieces = lax.all_to_all(pieces, "gy", 0, 0, tiled=True)
    coarse_block = pieces.reshape(cols_y * modes, rows_x * modes)

    def rounded_window(current):
        return extended(current.astype(jnp.bfloat16), (("gx", 0), ("gy", 1)), margin)

    def precondition(current):
        window = rounded_window(current).reshape(extent * extent, fields)
        local_part = jnp.dot(inverse_rows, window, preferred_element_type=jnp.float32)
        local_part = lax.optimization_barrier(local_part).reshape(patch, patch, fields)
        flat_core = current.reshape(patch * patch, fields)
        restricted = jnp.dot(flat_basis, flat_core, precision=highest)
        squares = jnp.sum(flat_core * flat_core, axis=0)
        carried = jnp.concatenate([restricted, squares[None]], axis=0)
        gathered = gathered_by_exchange(carried, "gx")
        column_total = jnp.sum(gathered[:, modes], axis=0)
        column_coarse = gathered[:, :modes].reshape(rows_x * modes, fields)
        partial = jnp.dot(coarse_block, column_coarse, precision=highest).reshape(
            cols_y, modes, fields
        )
        partial = jnp.concatenate(
            [partial, jnp.broadcast_to(column_total, (cols_y, 1, fields))], axis=1
        )
        reduced = summed_by_exchange(partial, "gy")
        coarse_part = reduced[:modes]
        squares_all = reduced[modes]
        prolonged = jnp.dot(flat_basis.T, coarse_part, precision=highest).reshape(
            patch, patch, fields
        )
        return (local_part + prolonged, squares_all)

    centre = 0.5 * (upper_bound + lower_bound)
    half_width = 0.5 * (upper_bound - lower_bound)
    relative = centre / half_width
    weight_prev = 1.0 / relative
    solution = jnp.zeros_like(sources)
    corrected, initial = precondition(state)
    history = []
    update = corrected / centre
    for index in range(ITERS):
        solution = solution + update
        step_pad = with_edges(update)
        state = state - operate(step_pad, kappa_pad, storage)
        if index + 1 < ITERS:
            corrected, squares = precondition(state)
            history.append(squares)
            weight_next = 1.0 / (2.0 * relative - weight_prev)
            update = weight_next * weight_prev * update + 2.0 * weight_next / half_width * corrected
            weight_prev = weight_next
        else:
            flat_state = state.reshape(patch * patch, fields)
            history.append(total_over_mesh(jnp.sum(flat_state * flat_state, axis=0)))
    return (solution, jnp.sqrt(jnp.stack(history) / cells), jnp.sqrt(initial / cells))


def solution(mesh):
    placed = (
        P("gx", "gy", None),
        P("gx", "gy"),
        P("gx", "gy"),
        P(None, "gx", "gy"),
        P("gx", "gy", None, None),
        P(("gx", "gy"), None),
    )
    return jax.shard_map(
        on_device,
        mesh=mesh,
        in_specs=placed,
        out_specs=(P("gx", "gy", None), P(), P()),
        check_vma=False,
    )
```

```python
import jax
import jax.numpy as jnp
from jax import lax
from jax.sharding import PartitionSpec as P

OV = 4
ITERS = 3


lower_bound = 0.15
upper_bound = 1.9
highest = lax.Precision.HIGHEST


def extended(cells, sides, width):
    for axis, dim in sides:
        count = lax.axis_size(axis)
        ends = count - 1
        head = lax.slice_in_dim(cells, 0, width, axis=dim)
        tail = lax.slice_in_dim(cells, cells.shape[dim] - width, cells.shape[dim], axis=dim)
        cells = jnp.concatenate(
            [
                lax.ppermute(tail, axis, [(i, (i + 1) % count) for i in range(ends)]),
                cells,
                lax.ppermute(head, axis, [((i + 1) % count, i) for i in range(ends)]),
            ],
            axis=dim,
        )
    return cells


def with_edges(cells):
    rows_x = lax.axis_size("gx")
    cols_y = lax.axis_size("gy")
    down = [(i, i + 1) for i in range(rows_x - 1)]
    up = [(i + 1, i) for i in range(rows_x - 1)]
    right = [(i, i + 1) for i in range(cols_y - 1)]
    left = [(i + 1, i) for i in range(cols_y - 1)]
    north = lax.ppermute(cells[-1:], "gx", down)
    south = lax.ppermute(cells[:1], "gx", up)
    west = lax.ppermute(cells[:, -1:], "gy", right)
    east = lax.ppermute(cells[:, :1], "gy", left)
    rows = jnp.concatenate([north, cells, south], axis=0)
    corner = [(1, 1), (0, 0)] + [(0, 0)] * (cells.ndim - 2)
    return jnp.concatenate(
        [jnp.pad(west, corner), rows, jnp.pad(east, corner)], axis=1
    )


def window_of(cells, width):
    rows_x = lax.axis_size("gx")
    cols_y = lax.axis_size("gy")
    down = [(i, i + 1) for i in range(rows_x - 1)]
    up = [(i + 1, i) for i in range(rows_x - 1)]
    right = [(i, i + 1) for i in range(cols_y - 1)]
    left = [(i + 1, i) for i in range(cols_y - 1)]

    def diagonal(step_x, step_y):
        pairs = []
        for a in range(rows_x):
            for b in range(cols_y):
                if 0 <= a + step_x < rows_x and 0 <= b + step_y < cols_y:
                    pairs.append((a * cols_y + b, (a + step_x) * cols_y + b + step_y))
        return pairs

    north = lax.ppermute(cells[-width:], "gx", down)
    south = lax.ppermute(cells[:width], "gx", up)
    west = lax.ppermute(cells[:, -width:], "gy", right)
    east = lax.ppermute(cells[:, :width], "gy", left)
    both = ("gx", "gy")
    north_west = lax.ppermute(cells[-width:, -width:], both, diagonal(1, 1))
    north_east = lax.ppermute(cells[-width:, :width], both, diagonal(1, -1))
    south_west = lax.ppermute(cells[:width, -width:], both, diagonal(-1, 1))
    south_east = lax.ppermute(cells[:width, :width], both, diagonal(-1, -1))
    top = jnp.concatenate([north_west, north, north_east], axis=1)
    middle = jnp.concatenate([west, cells, east], axis=1)
    bottom = jnp.concatenate([south_west, south, south_east], axis=1)
    return jnp.concatenate([top, middle, bottom], axis=0)


def neighbour(padded, offset_row, offset_col):
    inner_rows = padded.shape[0] - 2
    inner_cols = padded.shape[1] - 2
    return padded[
        1 + offset_row : 1 + offset_row + inner_rows, 1 + offset_col : 1 + offset_col + inner_cols
    ]


def operate(field_pad, kappa_pad, storage_used):
    centre = neighbour(field_pad, 0, 0)
    kappa = neighbour(kappa_pad, 0, 0)
    total = storage_used[:, :, None] * centre
    for offset_row, offset_col in ((1, 0), (-1, 0), (0, 1), (0, -1)):
        faces = 0.5 * (kappa + neighbour(kappa_pad, offset_row, offset_col))
        total = total + faces[:, :, None] * (centre - neighbour(field_pad, offset_row, offset_col))
    return total


def gathered_by_exchange(block, axis):
    count = lax.axis_size(axis)
    flat = block.reshape(-1)
    copies = jnp.broadcast_to(flat[None], (count, flat.shape[0]))
    return lax.all_to_all(copies, axis, 0, 0, tiled=True).reshape((count,) + block.shape)


def summed_by_exchange(blocks, axis):
    count = blocks.shape[0]
    flat = blocks.reshape(count, -1)
    received = lax.all_to_all(flat, axis, 0, 0, tiled=True)
    return jnp.sum(received, axis=0).reshape(blocks.shape[1:])


def total_over_mesh(values):
    return jnp.sum(gathered_by_exchange(values, ("gx", "gy")), axis=0)


def on_device(sources, permeability, storage, basis, local_inverse, coarse_inverse):
    patch = sources.shape[0]
    fields = sources.shape[2]
    modes = basis.shape[0]
    rows_x = lax.axis_size("gx")
    cols_y = lax.axis_size("gy")
    margin = OV
    extent = patch + 2 * margin
    cells = float(patch * patch * rows_x * cols_y)
    flat_basis = basis.reshape(modes, patch * patch)
    inverse_rows = local_inverse[0, 0]
    kappa_pad = with_edges(permeability)
    state = sources

    pieces = coarse_inverse.reshape(modes, rows_x, cols_y, modes).transpose(2, 0, 1, 3)
    pieces = lax.all_to_all(pieces, "gy", 0, 0, tiled=True)
    coarse_block = pieces.reshape(cols_y * modes, rows_x * modes)

    def rounded_window(current):
        return window_of(current.astype(jnp.bfloat16), margin)

    def precondition(current):
        window = rounded_window(current).reshape(extent * extent, fields)
        local_part = jnp.dot(inverse_rows, window, preferred_element_type=jnp.float32)
        local_part = lax.optimization_barrier(local_part).reshape(patch, patch, fields)
        flat_core = current.reshape(patch * patch, fields)
        restricted = jnp.dot(flat_basis, flat_core, precision=highest)
        squares = jnp.sum(flat_core * flat_core, axis=0)
        carried = jnp.concatenate([restricted, squares[None]], axis=0)
        gathered = gathered_by_exchange(carried, "gx")
        column_total = jnp.sum(gathered[:, modes], axis=0)
        column_coarse = gathered[:, :modes].reshape(rows_x * modes, fields)
        partial = jnp.dot(coarse_block, column_coarse, precision=highest).reshape(
            cols_y, modes, fields
        )
        partial = jnp.concatenate(
            [partial, jnp.broadcast_to(column_total, (cols_y, 1, fields))], axis=1
        )
        reduced = summed_by_exchange(partial, "gy")
        coarse_part = reduced[:modes]
        squares_all = reduced[modes]
        prolonged = jnp.dot(flat_basis.T, coarse_part, precision=highest).reshape(
            patch, patch, fields
        )
        return (local_part + prolonged, squares_all)

    centre = 0.5 * (upper_bound + lower_bound)
    half_width = 0.5 * (upper_bound - lower_bound)
    relative = centre / half_width
    weight_prev = 1.0 / relative
    solution = jnp.zeros_like(sources)
    corrected, initial = precondition(state)
    history = []
    update = corrected / centre
    for index in range(ITERS):
        solution = solution + update
        step_pad = with_edges(update)
        state = state - operate(step_pad, kappa_pad, storage)
        if index + 1 < ITERS:
            corrected, squares = precondition(state)
            history.append(squares)
            weight_next = 1.0 / (2.0 * relative - weight_prev)
            update = weight_next * weight_prev * update + 2.0 * weight_next / half_width * corrected
            weight_prev = weight_next
        else:
            flat_state = state.reshape(patch * patch, fields)
            history.append(total_over_mesh(jnp.sum(flat_state * flat_state, axis=0)))
    return (solution, jnp.sqrt(jnp.stack(history) / cells), jnp.sqrt(initial / cells))


def solution(mesh):
    placed = (
        P("gx", "gy", None),
        P("gx", "gy"),
        P("gx", "gy"),
        P(None, "gx", "gy"),
        P("gx", "gy", None, None),
        P(("gx", "gy"), None),
    )
    return jax.shard_map(
        on_device,
        mesh=mesh,
        in_specs=placed,
        out_specs=(P("gx", "gy", None), P(), P()),
        check_vma=False,
    )
```

```python
import jax
import jax.numpy as jnp
from jax import lax
from jax.sharding import PartitionSpec as P

OV = 4
ITERS = 3


lower_bound = 0.15
upper_bound = 1.9
highest = lax.Precision.HIGHEST


def extended(cells, sides, width):
    for axis, dim in sides:
        count = lax.axis_size(axis)
        ends = count - 1
        head = lax.slice_in_dim(cells, 0, width, axis=dim)
        tail = lax.slice_in_dim(cells, cells.shape[dim] - width, cells.shape[dim], axis=dim)
        cells = jnp.concatenate(
            [
                lax.ppermute(tail, axis, [(i, (i + 1) % count) for i in range(ends)]),
                cells,
                lax.ppermute(head, axis, [((i + 1) % count, i) for i in range(ends)]),
            ],
            axis=dim,
        )
    return cells


def with_edges(cells):
    rows_x = lax.axis_size("gx")
    cols_y = lax.axis_size("gy")
    down = [(i, i + 1) for i in range(rows_x - 1)]
    up = [(i + 1, i) for i in range(rows_x - 1)]
    right = [(i, i + 1) for i in range(cols_y - 1)]
    left = [(i + 1, i) for i in range(cols_y - 1)]
    north = lax.ppermute(cells[-1:], "gx", down)
    south = lax.ppermute(cells[:1], "gx", up)
    west = lax.ppermute(cells[:, -1:], "gy", right)
    east = lax.ppermute(cells[:, :1], "gy", left)
    rows = jnp.concatenate([north, cells, south], axis=0)
    corner = [(1, 1), (0, 0)] + [(0, 0)] * (cells.ndim - 2)
    return jnp.concatenate(
        [jnp.pad(west, corner), rows, jnp.pad(east, corner)], axis=1
    )


def neighbour(padded, offset_row, offset_col):
    inner_rows = padded.shape[0] - 2
    inner_cols = padded.shape[1] - 2
    return padded[
        1 + offset_row : 1 + offset_row + inner_rows, 1 + offset_col : 1 + offset_col + inner_cols
    ]


def operate(field_pad, kappa_pad, storage_used):
    centre = neighbour(field_pad, 0, 0)
    kappa = neighbour(kappa_pad, 0, 0)
    total = storage_used[:, :, None] * centre
    for offset_row, offset_col in ((1, 0), (-1, 0), (0, 1), (0, -1)):
        faces = 0.5 * (kappa + neighbour(kappa_pad, offset_row, offset_col))
        total = total + faces[:, :, None] * (centre - neighbour(field_pad, offset_row, offset_col))
    return total


def gathered_by_exchange(block, axis):
    count = lax.axis_size(axis)
    flat = block.reshape(-1)
    copies = jnp.broadcast_to(flat[None], (count, flat.shape[0]))
    return lax.all_to_all(copies, axis, 0, 0, tiled=True).reshape((count,) + block.shape)


def summed_by_exchange(blocks, axis):
    count = blocks.shape[0]
    flat = blocks.reshape(count, -1)
    received = lax.all_to_all(flat, axis, 0, 0, tiled=True)
    return jnp.sum(received, axis=0).reshape(blocks.shape[1:])


def total_over_mesh(values):
    return jnp.sum(gathered_by_exchange(values, ("gx", "gy")), axis=0)


def on_device(sources, permeability, storage, basis, local_inverse, coarse_inverse):
    patch = sources.shape[0]
    fields = sources.shape[2]
    modes = basis.shape[0]
    rows_x = lax.axis_size("gx")
    cols_y = lax.axis_size("gy")
    margin = OV
    extent = patch + 2 * margin
    cells = float(patch * patch * rows_x * cols_y)
    flat_basis = basis.reshape(modes, patch * patch)
    inverse_rows = local_inverse[0, 0]
    kappa_pad = with_edges(permeability)
    state = sources

    pieces = coarse_inverse.reshape(modes, rows_x, cols_y * modes).transpose(1, 0, 2)
    pieces = lax.all_to_all(pieces, "gx", 0, 0, tiled=True)
    coarse_block = pieces.reshape(rows_x * modes, cols_y * modes)

    def rounded_window(current):
        return extended(current.astype(jnp.bfloat16), (("gx", 0), ("gy", 1)), margin)

    def precondition(current):
        window = rounded_window(current).reshape(extent * extent, fields)
        local_part = jnp.dot(inverse_rows, window, preferred_element_type=jnp.float32)
        local_part = lax.optimization_barrier(local_part).reshape(patch, patch, fields)
        flat_core = current.reshape(patch * patch, fields)
        restricted = jnp.dot(flat_basis, flat_core, precision=highest)
        squares = jnp.sum(flat_core * flat_core, axis=0)
        carried = jnp.concatenate([restricted, squares[None]], axis=0)
        gathered = gathered_by_exchange(carried, "gy")
        row_total = jnp.sum(gathered[:, modes], axis=0)
        row_coarse = gathered[:, :modes].reshape(cols_y * modes, fields)
        partial = jnp.dot(coarse_block, row_coarse, precision=highest).reshape(
            rows_x, modes, fields
        )
        partial = jnp.concatenate(
            [partial, jnp.broadcast_to(row_total, (rows_x, 1, fields))], axis=1
        )
        reduced = summed_by_exchange(partial, "gx")
        coarse_part = reduced[:modes]
        squares_all = reduced[modes]
        prolonged = jnp.dot(flat_basis.T, coarse_part, precision=highest).reshape(
            patch, patch, fields
        )
        return (local_part + prolonged, squares_all)

    centre = 0.5 * (upper_bound + lower_bound)
    half_width = 0.5 * (upper_bound - lower_bound)
    relative = centre / half_width
    weight_prev = 1.0 / relative
    solution = jnp.zeros_like(sources)
    corrected, initial = precondition(state)
    history = []
    update = corrected / centre
    for index in range(ITERS):
        solution = solution + update
        step_pad = with_edges(update)
        state = state - operate(step_pad, kappa_pad, storage)
        if index + 1 < ITERS:
            corrected, squares = precondition(state)
            history.append(squares)
            weight_next = 1.0 / (2.0 * relative - weight_prev)
            update = weight_next * weight_prev * update + 2.0 * weight_next / half_width * corrected
            weight_prev = weight_next
        else:
            flat_state = state.reshape(patch * patch, fields)
            history.append(total_over_mesh(jnp.sum(flat_state * flat_state, axis=0)))
    return (solution, jnp.sqrt(jnp.stack(history) / cells), jnp.sqrt(initial / cells))


def solution(mesh):
    placed = (
        P("gx", "gy", None),
        P("gx", "gy"),
        P("gx", "gy"),
        P(None, "gx", "gy"),
        P("gx", "gy", None, None),
        P(("gx", "gy"), None),
    )
    return jax.shard_map(
        on_device,
        mesh=mesh,
        in_specs=placed,
        out_specs=(P("gx", "gy", None), P(), P()),
        check_vma=False,
    )
```

```python
import jax
import jax.numpy as jnp
from jax import lax
from jax.sharding import PartitionSpec as P

OV = 4
ITERS = 3


lower_bound = 0.15
upper_bound = 1.9
highest = lax.Precision.HIGHEST


def extended(cells, sides, width):
    for axis, dim in sides:
        count = lax.axis_size(axis)
        ends = count - 1
        head = lax.slice_in_dim(cells, 0, width, axis=dim)
        tail = lax.slice_in_dim(cells, cells.shape[dim] - width, cells.shape[dim], axis=dim)
        cells = jnp.concatenate(
            [
                lax.ppermute(tail, axis, [(i, (i + 1) % count) for i in range(ends)]),
                cells,
                lax.ppermute(head, axis, [((i + 1) % count, i) for i in range(ends)]),
            ],
            axis=dim,
        )
    return cells


def with_edges(cells):
    rows_x = lax.axis_size("gx")
    cols_y = lax.axis_size("gy")
    down = [(i, i + 1) for i in range(rows_x - 1)]
    up = [(i + 1, i) for i in range(rows_x - 1)]
    right = [(i, i + 1) for i in range(cols_y - 1)]
    left = [(i + 1, i) for i in range(cols_y - 1)]
    north = lax.ppermute(cells[-1:], "gx", down)
    south = lax.ppermute(cells[:1], "gx", up)
    west = lax.ppermute(cells[:, -1:], "gy", right)
    east = lax.ppermute(cells[:, :1], "gy", left)
    rows = jnp.concatenate([north, cells, south], axis=0)
    corner = [(1, 1), (0, 0)] + [(0, 0)] * (cells.ndim - 2)
    return jnp.concatenate(
        [jnp.pad(west, corner), rows, jnp.pad(east, corner)], axis=1
    )


def neighbour(padded, offset_row, offset_col):
    inner_rows = padded.shape[0] - 2
    inner_cols = padded.shape[1] - 2
    return padded[
        1 + offset_row : 1 + offset_row + inner_rows, 1 + offset_col : 1 + offset_col + inner_cols
    ]


def operate(field_pad, kappa_pad, storage_used):
    centre = neighbour(field_pad, 0, 0)
    kappa = neighbour(kappa_pad, 0, 0)
    total = storage_used[:, :, None] * centre
    for offset_row, offset_col in ((1, 0), (-1, 0), (0, 1), (0, -1)):
        faces = 0.5 * (kappa + neighbour(kappa_pad, offset_row, offset_col))
        total = total + faces[:, :, None] * (centre - neighbour(field_pad, offset_row, offset_col))
    return total


def gathered_by_exchange(block, axis):
    count = lax.axis_size(axis)
    flat = block.reshape(-1)
    copies = jnp.broadcast_to(flat[None], (count, flat.shape[0]))
    return lax.all_to_all(copies, axis, 0, 0, tiled=True).reshape((count,) + block.shape)


def summed_by_exchange(blocks, axis):
    count = blocks.shape[0]
    flat = blocks.reshape(count, -1)
    received = lax.all_to_all(flat, axis, 0, 0, tiled=True)
    return jnp.sum(received, axis=0).reshape(blocks.shape[1:])


def total_over_mesh(values):
    return jnp.sum(gathered_by_exchange(values, ("gx", "gy")), axis=0)


def on_device(sources, permeability, storage, basis, local_inverse, coarse_inverse):
    patch = sources.shape[0]
    fields = sources.shape[2]
    modes = basis.shape[0]
    rows_x = lax.axis_size("gx")
    cols_y = lax.axis_size("gy")
    margin = OV
    extent = patch + 2 * margin
    cells = float(patch * patch * rows_x * cols_y)
    flat_basis = basis.reshape(modes, patch * patch)
    inverse_rows = local_inverse[0, 0]
    kappa_pad = with_edges(permeability)
    state = sources

    pieces = coarse_inverse.reshape(modes, rows_x, cols_y * modes).transpose(1, 0, 2)
    pieces = lax.all_to_all(pieces, "gx", 0, 0, tiled=True)
    coarse_block = pieces.reshape(rows_x * modes, cols_y * modes)

    def rounded_window(current):
        return extended(current.astype(jnp.bfloat16), (("gx", 0), ("gy", 1)), margin)

    def precondition(current):
        window = rounded_window(current).reshape(extent * extent, fields)
        local_part = jnp.dot(inverse_rows, window, preferred_element_type=jnp.float32)
        local_part = lax.optimization_barrier(local_part).reshape(patch, patch, fields)
        flat_core = current.reshape(patch * patch, fields)
        restricted = jnp.dot(flat_basis, flat_core, precision=highest)
        squares = jnp.sum(flat_core * flat_core, axis=0)
        carried = jnp.concatenate([restricted, squares[None]], axis=0)
        gathered = gathered_by_exchange(carried, "gy")
        row_total = jnp.sum(gathered[:, modes], axis=0)
        row_coarse = gathered[:, :modes].reshape(cols_y * modes, fields)
        partial = jnp.dot(coarse_block, row_coarse, precision=highest).reshape(
            rows_x, modes, fields
        )
        coarse_part = summed_by_exchange(partial, "gx")
        prolonged = jnp.dot(flat_basis.T, coarse_part, precision=highest).reshape(
            patch, patch, fields
        )
        return (local_part + prolonged, row_total)

    centre = 0.5 * (upper_bound + lower_bound)
    half_width = 0.5 * (upper_bound - lower_bound)
    relative = centre / half_width
    weight_prev = 1.0 / relative
    solution = jnp.zeros_like(sources)
    corrected, initial = precondition(state)
    history = []
    update = corrected / centre
    for index in range(ITERS):
        solution = solution + update
        step_pad = with_edges(update)
        state = state - operate(step_pad, kappa_pad, storage)
        if index + 1 < ITERS:
            corrected, squares = precondition(state)
            history.append(squares)
            weight_next = 1.0 / (2.0 * relative - weight_prev)
            update = weight_next * weight_prev * update + 2.0 * weight_next / half_width * corrected
            weight_prev = weight_next
        else:
            flat_state = state.reshape(patch * patch, fields)
            last = jnp.sum(flat_state * flat_state, axis=0)
            history.append(jnp.sum(gathered_by_exchange(last, "gy"), axis=0))
    rows = jnp.stack([initial] + history)
    totals = jnp.sum(gathered_by_exchange(rows, "gx"), axis=0)
    return (solution, jnp.sqrt(totals[1:] / cells), jnp.sqrt(totals[0] / cells))


def solution(mesh):
    placed = (
        P("gx", "gy", None),
        P("gx", "gy"),
        P("gx", "gy"),
        P(None, "gx", "gy"),
        P("gx", "gy", None, None),
        P(("gx", "gy"), None),
    )
    return jax.shard_map(
        on_device,
        mesh=mesh,
        in_specs=placed,
        out_specs=(P("gx", "gy", None), P(), P()),
        check_vma=False,
    )
```

```python
import jax
import jax.numpy as jnp
from jax import lax
from jax.sharding import PartitionSpec as P

OV = 4
ITERS = 3


lower_bound = 0.15
upper_bound = 1.9
highest = lax.Precision.HIGHEST


def extended(cells, sides, width):
    for axis, dim in sides:
        count = lax.axis_size(axis)
        ends = count - 1
        head = lax.slice_in_dim(cells, 0, width, axis=dim)
        tail = lax.slice_in_dim(cells, cells.shape[dim] - width, cells.shape[dim], axis=dim)
        cells = jnp.concatenate(
            [
                lax.ppermute(tail, axis, [(i, (i + 1) % count) for i in range(ends)]),
                cells,
                lax.ppermute(head, axis, [((i + 1) % count, i) for i in range(ends)]),
            ],
            axis=dim,
        )
    return cells


def with_edges(cells):
    rows_x = lax.axis_size("gx")
    cols_y = lax.axis_size("gy")
    down = [(i, i + 1) for i in range(rows_x - 1)]
    up = [(i + 1, i) for i in range(rows_x - 1)]
    right = [(i, i + 1) for i in range(cols_y - 1)]
    left = [(i + 1, i) for i in range(cols_y - 1)]
    north = lax.ppermute(cells[-1:], "gx", down)
    south = lax.ppermute(cells[:1], "gx", up)
    west = lax.ppermute(cells[:, -1:], "gy", right)
    east = lax.ppermute(cells[:, :1], "gy", left)
    rows = jnp.concatenate([north, cells, south], axis=0)
    corner = [(1, 1), (0, 0)] + [(0, 0)] * (cells.ndim - 2)
    return jnp.concatenate(
        [jnp.pad(west, corner), rows, jnp.pad(east, corner)], axis=1
    )


def neighbour(padded, offset_row, offset_col):
    inner_rows = padded.shape[0] - 2
    inner_cols = padded.shape[1] - 2
    return padded[
        1 + offset_row : 1 + offset_row + inner_rows, 1 + offset_col : 1 + offset_col + inner_cols
    ]


def operate(field_pad, kappa_pad, storage_used):
    centre = neighbour(field_pad, 0, 0)
    kappa = neighbour(kappa_pad, 0, 0)
    total = storage_used[:, :, None] * centre
    for offset_row, offset_col in ((1, 0), (-1, 0), (0, 1), (0, -1)):
        faces = 0.5 * (kappa + neighbour(kappa_pad, offset_row, offset_col))
        total = total + faces[:, :, None] * (centre - neighbour(field_pad, offset_row, offset_col))
    return total


def gathered_by_exchange(block, axis):
    count = lax.axis_size(axis)
    flat = block.reshape(-1)
    copies = jnp.broadcast_to(flat[None], (count, flat.shape[0]))
    return lax.all_to_all(copies, axis, 0, 0, tiled=True).reshape((count,) + block.shape)


def summed_by_exchange(blocks, axis):
    count = blocks.shape[0]
    flat = blocks.reshape(count, -1)
    received = lax.all_to_all(flat, axis, 0, 0, tiled=True)
    return jnp.sum(received, axis=0).reshape(blocks.shape[1:])


def total_over_mesh(values):
    return jnp.sum(gathered_by_exchange(values, ("gx", "gy")), axis=0)


def on_device(sources, permeability, storage, basis, local_inverse, coarse_inverse):
    patch = sources.shape[0]
    fields = sources.shape[2]
    modes = basis.shape[0]
    rows_x = lax.axis_size("gx")
    cols_y = lax.axis_size("gy")
    margin = OV
    extent = patch + 2 * margin
    cells = float(patch * patch * rows_x * cols_y)
    flat_basis = basis.reshape(modes, patch * patch)
    inverse_rows = local_inverse[0, 0]
    kappa_pad = with_edges(permeability)
    state = sources

    pieces = coarse_inverse.reshape(modes, rows_x, cols_y * modes).transpose(1, 0, 2)
    pieces = lax.all_to_all(pieces, "gx", 0, 0, tiled=True)
    coarse_block = pieces.reshape(rows_x * modes, cols_y * modes)

    def rounded_window(current):
        return extended(current.astype(jnp.bfloat16), (("gx", 0), ("gy", 1)), margin)

    def precondition(current):
        window = rounded_window(current).reshape(extent * extent, fields)
        local_part = jnp.dot(inverse_rows, window, preferred_element_type=jnp.float32)
        local_part = lax.optimization_barrier(local_part).reshape(patch, patch, fields)
        flat_core = current.reshape(patch * patch, fields)
        restricted = jnp.dot(flat_basis, flat_core, precision=highest)
        squares = jnp.sum(flat_core * flat_core, axis=0)
        carried = jnp.concatenate([restricted, squares[None]], axis=0)
        gathered = gathered_by_exchange(carried, "gy")
        row_total = jnp.sum(gathered[:, modes], axis=0)
        row_coarse = gathered[:, :modes].reshape(cols_y * modes, fields)
        partial = jnp.dot(coarse_block, row_coarse, precision=highest).reshape(
            rows_x, modes, fields
        )
        coarse_part = summed_by_exchange(partial, "gx")
        prolonged = basis[0][:, :, None] * coarse_part[0]
        for mode in range(1, modes):
            prolonged = prolonged + basis[mode][:, :, None] * coarse_part[mode]
        return (local_part + prolonged, row_total)

    centre = 0.5 * (upper_bound + lower_bound)
    half_width = 0.5 * (upper_bound - lower_bound)
    relative = centre / half_width
    weight_prev = 1.0 / relative
    solution = jnp.zeros_like(sources)
    corrected, initial = precondition(state)
    history = []
    update = corrected / centre
    for index in range(ITERS):
        solution = solution + update
        step_pad = with_edges(update)
        state = state - operate(step_pad, kappa_pad, storage)
        if index + 1 < ITERS:
            corrected, squares = precondition(state)
            history.append(squares)
            weight_next = 1.0 / (2.0 * relative - weight_prev)
            update = weight_next * weight_prev * update + 2.0 * weight_next / half_width * corrected
            weight_prev = weight_next
        else:
            flat_state = state.reshape(patch * patch, fields)
            last = jnp.sum(flat_state * flat_state, axis=0)
            history.append(jnp.sum(gathered_by_exchange(last, "gy"), axis=0))
    rows = jnp.stack([initial] + history)
    totals = jnp.sum(gathered_by_exchange(rows, "gx"), axis=0)
    return (solution, jnp.sqrt(totals[1:] / cells), jnp.sqrt(totals[0] / cells))


def solution(mesh):
    placed = (
        P("gx", "gy", None),
        P("gx", "gy"),
        P("gx", "gy"),
        P(None, "gx", "gy"),
        P("gx", "gy", None, None),
        P(("gx", "gy"), None),
    )
    return jax.shard_map(
        on_device,
        mesh=mesh,
        in_specs=placed,
        out_specs=(P("gx", "gy", None), P(), P()),
        check_vma=False,
    )
```

```python
import jax
import jax.numpy as jnp
from jax import lax
from jax.sharding import PartitionSpec as P

OV = 4
ITERS = 3


lower_bound = 0.15
upper_bound = 1.9
highest = lax.Precision.HIGHEST


def extended(cells, sides, width):
    for axis, dim in sides:
        count = lax.axis_size(axis)
        ends = count - 1
        head = lax.slice_in_dim(cells, 0, width, axis=dim)
        tail = lax.slice_in_dim(cells, cells.shape[dim] - width, cells.shape[dim], axis=dim)
        cells = jnp.concatenate(
            [
                lax.ppermute(tail, axis, [(i, (i + 1) % count) for i in range(ends)]),
                cells,
                lax.ppermute(head, axis, [((i + 1) % count, i) for i in range(ends)]),
            ],
            axis=dim,
        )
    return cells


def with_edges(cells):
    rows_x = lax.axis_size("gx")
    cols_y = lax.axis_size("gy")
    down = [(i, i + 1) for i in range(rows_x - 1)]
    up = [(i + 1, i) for i in range(rows_x - 1)]
    right = [(i, i + 1) for i in range(cols_y - 1)]
    left = [(i + 1, i) for i in range(cols_y - 1)]
    north = lax.ppermute(cells[-1:], "gx", down)
    south = lax.ppermute(cells[:1], "gx", up)
    west = lax.ppermute(cells[:, -1:], "gy", right)
    east = lax.ppermute(cells[:, :1], "gy", left)
    rows = jnp.concatenate([north, cells, south], axis=0)
    corner = [(1, 1), (0, 0)] + [(0, 0)] * (cells.ndim - 2)
    return jnp.concatenate(
        [jnp.pad(west, corner), rows, jnp.pad(east, corner)], axis=1
    )


def neighbour(padded, offset_row, offset_col):
    inner_rows = padded.shape[0] - 2
    inner_cols = padded.shape[1] - 2
    return padded[
        1 + offset_row : 1 + offset_row + inner_rows, 1 + offset_col : 1 + offset_col + inner_cols
    ]


def operate(field_pad, kappa_pad, storage_used):
    centre = neighbour(field_pad, 0, 0)
    kappa = neighbour(kappa_pad, 0, 0)
    total = storage_used[:, :, None] * centre
    for offset_row, offset_col in ((1, 0), (-1, 0), (0, 1), (0, -1)):
        faces = 0.5 * (kappa + neighbour(kappa_pad, offset_row, offset_col))
        total = total + faces[:, :, None] * (centre - neighbour(field_pad, offset_row, offset_col))
    return total


def gathered_by_exchange(block, axis):
    count = lax.axis_size(axis)
    flat = block.reshape(-1)
    copies = jnp.broadcast_to(flat[None], (count, flat.shape[0]))
    return lax.all_to_all(copies, axis, 0, 0, tiled=True).reshape((count,) + block.shape)


def summed_by_exchange(blocks, axis):
    count = blocks.shape[0]
    flat = blocks.reshape(count, -1)
    received = lax.all_to_all(flat, axis, 0, 0, tiled=True)
    return jnp.sum(received, axis=0).reshape(blocks.shape[1:])


def total_over_mesh(values):
    return jnp.sum(gathered_by_exchange(values, ("gx", "gy")), axis=0)


def on_device(sources, permeability, storage, basis, local_inverse, coarse_inverse):
    patch = sources.shape[0]
    fields = sources.shape[2]
    modes = basis.shape[0]
    rows_x = lax.axis_size("gx")
    cols_y = lax.axis_size("gy")
    margin = OV
    extent = patch + 2 * margin
    cells = float(patch * patch * rows_x * cols_y)
    flat_basis = basis.reshape(modes, patch * patch)
    inverse_rows = local_inverse[0, 0]
    kappa_pad = with_edges(permeability)
    state = sources

    pieces = coarse_inverse.reshape(modes, rows_x, cols_y * modes).transpose(1, 0, 2)
    pieces = lax.all_to_all(pieces, "gx", 0, 0, tiled=True)
    pieces, state = lax.optimization_barrier((pieces, state))
    coarse_block = pieces.reshape(rows_x * modes, cols_y * modes)

    def rounded_window(current):
        return extended(current.astype(jnp.bfloat16), (("gx", 0), ("gy", 1)), margin)

    def precondition(current):
        window = rounded_window(current).reshape(extent * extent, fields)
        local_part = jnp.dot(inverse_rows, window, preferred_element_type=jnp.float32)
        local_part = lax.optimization_barrier(local_part).reshape(patch, patch, fields)
        flat_core = current.reshape(patch * patch, fields)
        restricted = jnp.dot(flat_basis, flat_core, precision=highest)
        squares = jnp.sum(flat_core * flat_core, axis=0)
        carried = jnp.concatenate([restricted, squares[None]], axis=0)
        gathered = gathered_by_exchange(carried, "gy")
        row_total = jnp.sum(gathered[:, modes], axis=0)
        row_coarse = gathered[:, :modes].reshape(cols_y * modes, fields)
        partial = jnp.dot(coarse_block, row_coarse, precision=highest).reshape(
            rows_x, modes, fields
        )
        coarse_part = summed_by_exchange(partial, "gx")
        prolonged = basis[0][:, :, None] * coarse_part[0]
        for mode in range(1, modes):
            prolonged = prolonged + basis[mode][:, :, None] * coarse_part[mode]
        return (local_part + prolonged, row_total)

    centre = 0.5 * (upper_bound + lower_bound)
    half_width = 0.5 * (upper_bound - lower_bound)
    relative = centre / half_width
    weight_prev = 1.0 / relative
    solution = jnp.zeros_like(sources)
    corrected, initial = precondition(state)
    history = []
    update = corrected / centre
    for index in range(ITERS):
        solution = solution + update
        step_pad = with_edges(update)
        state = state - operate(step_pad, kappa_pad, storage)
        if index + 1 < ITERS:
            corrected, squares = precondition(state)
            history.append(squares)
            weight_next = 1.0 / (2.0 * relative - weight_prev)
            update = weight_next * weight_prev * update + 2.0 * weight_next / half_width * corrected
            weight_prev = weight_next
        else:
            flat_state = state.reshape(patch * patch, fields)
            last = jnp.sum(flat_state * flat_state, axis=0)
            history.append(jnp.sum(gathered_by_exchange(last, "gy"), axis=0))
    rows = jnp.stack([initial] + history)
    totals = jnp.sum(gathered_by_exchange(rows, "gx"), axis=0)
    return (solution, jnp.sqrt(totals[1:] / cells), jnp.sqrt(totals[0] / cells))


def solution(mesh):
    placed = (
        P("gx", "gy", None),
        P("gx", "gy"),
        P("gx", "gy"),
        P(None, "gx", "gy"),
        P("gx", "gy", None, None),
        P(("gx", "gy"), None),
    )
    return jax.shard_map(
        on_device,
        mesh=mesh,
        in_specs=placed,
        out_specs=(P("gx", "gy", None), P(), P()),
        check_vma=False,
    )
```

```python
import jax
import jax.numpy as jnp
from jax import lax
from jax.sharding import PartitionSpec as P

OV = 4
ITERS = 3


lower_bound = 0.15
upper_bound = 1.9
highest = lax.Precision.HIGHEST


def extended(cells, sides, width):
    for axis, dim in sides:
        count = lax.axis_size(axis)
        ends = count - 1
        head = lax.slice_in_dim(cells, 0, width, axis=dim)
        tail = lax.slice_in_dim(cells, cells.shape[dim] - width, cells.shape[dim], axis=dim)
        cells = jnp.concatenate(
            [
                lax.ppermute(tail, axis, [(i, (i + 1) % count) for i in range(ends)]),
                cells,
                lax.ppermute(head, axis, [((i + 1) % count, i) for i in range(ends)]),
            ],
            axis=dim,
        )
    return cells


def with_edges(cells):
    rows_x = lax.axis_size("gx")
    cols_y = lax.axis_size("gy")
    down = [(i, i + 1) for i in range(rows_x - 1)]
    up = [(i + 1, i) for i in range(rows_x - 1)]
    right = [(i, i + 1) for i in range(cols_y - 1)]
    left = [(i + 1, i) for i in range(cols_y - 1)]
    north = lax.ppermute(cells[-1:], "gx", down)
    south = lax.ppermute(cells[:1], "gx", up)
    west = lax.ppermute(cells[:, -1:], "gy", right)
    east = lax.ppermute(cells[:, :1], "gy", left)
    rows = jnp.concatenate([north, cells, south], axis=0)
    corner = [(1, 1), (0, 0)] + [(0, 0)] * (cells.ndim - 2)
    return jnp.concatenate(
        [jnp.pad(west, corner), rows, jnp.pad(east, corner)], axis=1
    )


def neighbour(padded, offset_row, offset_col):
    inner_rows = padded.shape[0] - 2
    inner_cols = padded.shape[1] - 2
    return padded[
        1 + offset_row : 1 + offset_row + inner_rows, 1 + offset_col : 1 + offset_col + inner_cols
    ]


def operate(field_pad, kappa_pad, storage_used):
    centre = neighbour(field_pad, 0, 0)
    kappa = neighbour(kappa_pad, 0, 0)
    total = storage_used[:, :, None] * centre
    for offset_row, offset_col in ((1, 0), (-1, 0), (0, 1), (0, -1)):
        faces = 0.5 * (kappa + neighbour(kappa_pad, offset_row, offset_col))
        total = total + faces[:, :, None] * (centre - neighbour(field_pad, offset_row, offset_col))
    return total


def gathered_by_exchange(block, axis):
    count = lax.axis_size(axis)
    flat = block.reshape(-1)
    copies = jnp.broadcast_to(flat[None], (count, flat.shape[0]))
    return lax.all_to_all(copies, axis, 0, 0, tiled=True).reshape((count,) + block.shape)


def summed_by_exchange(blocks, axis):
    count = blocks.shape[0]
    flat = blocks.reshape(count, -1)
    received = lax.all_to_all(flat, axis, 0, 0, tiled=True)
    return jnp.sum(received, axis=0).reshape(blocks.shape[1:])


def total_over_mesh(values):
    return jnp.sum(gathered_by_exchange(values, ("gx", "gy")), axis=0)


def on_device(sources, permeability, storage, basis, local_inverse, coarse_inverse):
    patch = sources.shape[0]
    fields = sources.shape[2]
    modes = basis.shape[0]
    rows_x = lax.axis_size("gx")
    cols_y = lax.axis_size("gy")
    margin = OV
    extent = patch + 2 * margin
    cells = float(patch * patch * rows_x * cols_y)
    flat_basis = basis.reshape(modes, patch * patch)
    inverse_rows = local_inverse[0, 0]
    kappa_pad = with_edges(permeability)
    state = sources

    pieces = coarse_inverse.reshape(modes, rows_x, cols_y * modes).transpose(1, 0, 2)
    pieces = lax.all_to_all(pieces, "gx", 0, 0, tiled=True)
    pieces, state = lax.optimization_barrier((pieces, state))
    coarse_block = pieces.reshape(rows_x * modes, cols_y * modes)

    def rounded_window(current):
        return extended(current.astype(jnp.bfloat16), (("gx", 0), ("gy", 1)), margin)

    def precondition(current):
        window = rounded_window(current).reshape(extent * extent, fields)
        local_part = jnp.dot(inverse_rows, window, preferred_element_type=jnp.float32)
        local_part = lax.optimization_barrier(local_part).reshape(patch, patch, fields)
        flat_core = current.reshape(patch * patch, fields)
        restricted = jnp.dot(flat_basis, flat_core, precision=highest)
        squares = jnp.sum(flat_core * flat_core, axis=0)
        gathered = gathered_by_exchange(restricted, "gy")
        row_coarse = gathered.reshape(cols_y * modes, fields)
        partial = jnp.dot(coarse_block, row_coarse, precision=highest).reshape(
            rows_x, modes, fields
        )
        coarse_part = summed_by_exchange(partial, "gx")
        prolonged = basis[0][:, :, None] * coarse_part[0]
        for mode in range(1, modes):
            prolonged = prolonged + basis[mode][:, :, None] * coarse_part[mode]
        return (local_part + prolonged, squares)

    centre = 0.5 * (upper_bound + lower_bound)
    half_width = 0.5 * (upper_bound - lower_bound)
    relative = centre / half_width
    weight_prev = 1.0 / relative
    solution = jnp.zeros_like(sources)
    corrected, initial = precondition(state)
    history = []
    update = corrected / centre
    for index in range(ITERS):
        solution = solution + update
        step_pad = with_edges(update)
        state = state - operate(step_pad, kappa_pad, storage)
        if index + 1 < ITERS:
            corrected, squares = precondition(state)
            history.append(squares)
            weight_next = 1.0 / (2.0 * relative - weight_prev)
            update = weight_next * weight_prev * update + 2.0 * weight_next / half_width * corrected
            weight_prev = weight_next
        else:
            flat_state = state.reshape(patch * patch, fields)
            last = jnp.sum(flat_state * flat_state, axis=0)
            history.append(last)
    rows = jnp.stack([initial] + history)
    rows = jnp.sum(gathered_by_exchange(rows, "gy"), axis=0)
    totals = jnp.sum(gathered_by_exchange(rows, "gx"), axis=0)
    return (solution, jnp.sqrt(totals[1:] / cells), jnp.sqrt(totals[0] / cells))


def solution(mesh):
    placed = (
        P("gx", "gy", None),
        P("gx", "gy"),
        P("gx", "gy"),
        P(None, "gx", "gy"),
        P("gx", "gy", None, None),
        P(("gx", "gy"), None),
    )
    return jax.shard_map(
        on_device,
        mesh=mesh,
        in_specs=placed,
        out_specs=(P("gx", "gy", None), P(), P()),
        check_vma=False,
    )
```

```python
import jax
import jax.numpy as jnp
from jax import lax
from jax.sharding import PartitionSpec as P

OV = 4
ITERS = 3


lower_bound = 0.15
upper_bound = 1.9
highest = lax.Precision.HIGHEST


def extended(cells, sides, width):
    for axis, dim in sides:
        count = lax.axis_size(axis)
        ends = count - 1
        head = lax.slice_in_dim(cells, 0, width, axis=dim)
        tail = lax.slice_in_dim(cells, cells.shape[dim] - width, cells.shape[dim], axis=dim)
        cells = jnp.concatenate(
            [
                lax.ppermute(tail, axis, [(i, (i + 1) % count) for i in range(ends)]),
                cells,
                lax.ppermute(head, axis, [((i + 1) % count, i) for i in range(ends)]),
            ],
            axis=dim,
        )
    return cells


def with_edges(cells):
    rows_x = lax.axis_size("gx")
    cols_y = lax.axis_size("gy")
    down = [(i, i + 1) for i in range(rows_x - 1)]
    up = [(i + 1, i) for i in range(rows_x - 1)]
    right = [(i, i + 1) for i in range(cols_y - 1)]
    left = [(i + 1, i) for i in range(cols_y - 1)]
    north = lax.ppermute(cells[-1:], "gx", down)
    south = lax.ppermute(cells[:1], "gx", up)
    west = lax.ppermute(cells[:, -1:], "gy", right)
    east = lax.ppermute(cells[:, :1], "gy", left)
    rows = jnp.concatenate([north, cells, south], axis=0)
    corner = [(1, 1), (0, 0)] + [(0, 0)] * (cells.ndim - 2)
    return jnp.concatenate(
        [jnp.pad(west, corner), rows, jnp.pad(east, corner)], axis=1
    )


def neighbour(padded, offset_row, offset_col):
    inner_rows = padded.shape[0] - 2
    inner_cols = padded.shape[1] - 2
    return padded[
        1 + offset_row : 1 + offset_row + inner_rows, 1 + offset_col : 1 + offset_col + inner_cols
    ]


def operate(field_pad, kappa_pad, storage_used):
    centre = neighbour(field_pad, 0, 0)
    kappa = neighbour(kappa_pad, 0, 0)
    total = storage_used[:, :, None] * centre
    for offset_row, offset_col in ((1, 0), (-1, 0), (0, 1), (0, -1)):
        faces = 0.5 * (kappa + neighbour(kappa_pad, offset_row, offset_col))
        total = total + faces[:, :, None] * (centre - neighbour(field_pad, offset_row, offset_col))
    return total


def gathered_by_exchange(block, axis):
    count = lax.axis_size(axis)
    flat = block.reshape(-1)
    copies = jnp.broadcast_to(flat[None], (count, flat.shape[0]))
    return lax.all_to_all(copies, axis, 0, 0, tiled=True).reshape((count,) + block.shape)


def summed_by_exchange(blocks, axis):
    count = blocks.shape[0]
    flat = blocks.reshape(count, -1)
    received = lax.all_to_all(flat, axis, 0, 0, tiled=True)
    return jnp.sum(received, axis=0).reshape(blocks.shape[1:])


def total_over_mesh(values):
    return jnp.sum(gathered_by_exchange(values, ("gx", "gy")), axis=0)


def on_device(sources, permeability, storage, basis, local_inverse, coarse_inverse):
    patch = sources.shape[0]
    fields = sources.shape[2]
    modes = basis.shape[0]
    rows_x = lax.axis_size("gx")
    cols_y = lax.axis_size("gy")
    margin = OV
    extent = patch + 2 * margin
    cells = float(patch * patch * rows_x * cols_y)
    flat_basis = basis.reshape(modes, patch * patch)
    inverse_rows = local_inverse[0, 0]
    kappa_pad = with_edges(permeability)
    state = sources

    pieces = coarse_inverse.reshape(modes, rows_x, cols_y * modes).transpose(1, 0, 2)
    pieces = lax.all_to_all(pieces, "gx", 0, 0, tiled=True)
    pieces, state = lax.optimization_barrier((pieces, state))
    coarse_block = pieces.reshape(rows_x * modes, cols_y * modes)

    def rounded_window(current):
        return extended(current.astype(jnp.bfloat16), (("gy", 1), ("gx", 0)), margin)

    def precondition(current):
        window = rounded_window(current).reshape(extent * extent, fields)
        local_part = jnp.dot(inverse_rows, window, preferred_element_type=jnp.float32)
        local_part = lax.optimization_barrier(local_part).reshape(patch, patch, fields)
        flat_core = current.reshape(patch * patch, fields)
        restricted = jnp.dot(flat_basis, flat_core, precision=highest)
        squares = jnp.sum(flat_core * flat_core, axis=0)
        gathered = gathered_by_exchange(restricted, "gy")
        row_coarse = gathered.reshape(cols_y * modes, fields)
        partial = jnp.dot(coarse_block, row_coarse, precision=highest).reshape(
            rows_x, modes, fields
        )
        coarse_part = summed_by_exchange(partial, "gx")
        prolonged = basis[0][:, :, None] * coarse_part[0]
        for mode in range(1, modes):
            prolonged = prolonged + basis[mode][:, :, None] * coarse_part[mode]
        return (local_part + prolonged, squares)

    centre = 0.5 * (upper_bound + lower_bound)
    half_width = 0.5 * (upper_bound - lower_bound)
    relative = centre / half_width
    weight_prev = 1.0 / relative
    solution = jnp.zeros_like(sources)
    corrected, initial = precondition(state)
    history = []
    update = corrected / centre
    for index in range(ITERS):
        solution = solution + update
        step_pad = with_edges(update)
        state = state - operate(step_pad, kappa_pad, storage)
        if index + 1 < ITERS:
            corrected, squares = precondition(state)
            history.append(squares)
            weight_next = 1.0 / (2.0 * relative - weight_prev)
            update = weight_next * weight_prev * update + 2.0 * weight_next / half_width * corrected
            weight_prev = weight_next
        else:
            flat_state = state.reshape(patch * patch, fields)
            last = jnp.sum(flat_state * flat_state, axis=0)
            history.append(last)
    rows = jnp.stack([initial] + history)
    rows = jnp.sum(gathered_by_exchange(rows, "gy"), axis=0)
    totals = jnp.sum(gathered_by_exchange(rows, "gx"), axis=0)
    return (solution, jnp.sqrt(totals[1:] / cells), jnp.sqrt(totals[0] / cells))


def solution(mesh):
    placed = (
        P("gx", "gy", None),
        P("gx", "gy"),
        P("gx", "gy"),
        P(None, "gx", "gy"),
        P("gx", "gy", None, None),
        P(("gx", "gy"), None),
    )
    return jax.shard_map(
        on_device,
        mesh=mesh,
        in_specs=placed,
        out_specs=(P("gx", "gy", None), P(), P()),
        check_vma=False,
    )
```
